512 devices in a mesh: expert: 8 (over y, core), mp: 64 (over x, z).
Axes of the slice: x: 4, y: 4, z: 16, core: 2. Of those that a mesh axis runs over, the one named last changes fastest.
Arguments:
- context: bfloat16 [4096, 2048], P('expert', 'mp'), may hold values from -6 to 6
- out_proj: bfloat16 [2048, 2048], P('mp'), may hold values from -1 to 1, as said below
- routes: int32 [4096, 2], P('expert'), may hold values from 0 to 7, all different within a row; in each aligned block of 512 rows (0 to 511, 512 to 1023, ...) at most 256 rows name the same one
- router_logits: float32 [4096, 2], P('expert'), may hold values from -8 to 8
- w_gate: bfloat16 [45056, 2048], P('mp', 'expert'), may hold values from -0.125 to 0.125
- w_up: bfloat16 [45056, 2048], P('mp', 'expert'), may hold values from -0.125 to 0.125
- w_down: bfloat16 [45056, 2048], P('mp', 'expert'), may hold values from -0.078125 to 0.078125
- norm_gain: float32 [2048], P('mp'), may hold values from 0.25 to 1.75
- request_order: int32 [4096], P('expert'), may hold values from 0 to 4095, each once
Outputs:
- restored: bfloat16 [4096, 2048], P('expert', 'mp')
The draws below stay inside these ranges and needn't reach their ends.
Inputs may be any that keep to these rules, and one draw needn't show every extreme that they name: `routes`: each row names 2 different experts. Within each aligned block of 512 rows no expert is named by more than 256 rows, and in some blocks one expert is named by exactly 256 rows. `request_order`: A permutation of the 4096 token rows. `out_proj`: entries of the order of one over the square root of 2048.
All inputs are finite; a program needn't handle non-finite values.
Results may differ from the reference program's by a relative error of at most 0.0056.
Values may be sent and summed in bfloat16 or wider, within the bound.
No kernel may reach another device: no remote copies, remote signals or barrier semaphores. Data moves between devices by JAX's collectives and lax.ppermute only.
A program may use at most 64 MiB of HBM per device.

```python
import math
import jax
import jax.numpy as jnp
import numpy as np
from jax import lax

D = 2048
FF = 5632
EXPERTS = 8
TOP = 2
TOK_DEV = 512
CAP = 256
TOKENS = 4096
N_EXPERT = 8


def draw_out_proj(key, part):
    position = jnp.arange(D, dtype=jnp.float32) / (D - 1)
    entries = jax.random.normal(key, (D, D), jnp.float32)
    row_scale = 0.3 * jnp.exp(math.log(10.0) * position)
    return (entries * row_scale[:, None] / math.sqrt(D)).astype(jnp.bfloat16)


def block_scale(own_key, extent, cuts, smallest, high):
    loudness = 1.0
    for axis_at, shards_of in cuts:
        draws = jax.random.uniform(jax.random.fold_in(jax.random.fold_in(own_key, 6), axis_at), (shards_of,), jnp.float32, smallest / len(cuts), high / len(cuts))
        loudness = loudness * jnp.repeat(jnp.exp(draws), extent[axis_at] // shards_of).reshape((-1,) + (1,) * (len(extent) - 1 - axis_at))
    return loudness


def routed_block(key, own, number, rows, count, top, most, skew):
    order = jax.random.permutation(key, count)
    crowded, ordinary = portions_of(count, rows * top, most, skew, True), portions_of(count, rows * top, most, skew, False)
    places = jnp.arange(count)

    def named(lengths, turn):
        used = int((lengths > 0).sum())
        fixed = max(1, used // 4)
        passed = fixed + (places - fixed + turn * (used - fixed)) % max(1, count - fixed)
        return jnp.zeros((count,), jnp.int32).at[order[jnp.where(places < fixed, places, passed)]].set(jnp.asarray(lengths, jnp.int32))

    lengths = jnp.where(number % 4 == 0, named(crowded, number // 4), named(ordinary, number - number // 4 - 1))
    mixed = jax.random.permutation(jax.random.fold_in(own, 3), count)
    donor, sink = mixed[0:count // 2 * 2:2], mixed[1:count // 2 * 2:2]
    room = jnp.minimum(lengths[donor] - 1, most - lengths[sink]) // 2
    room = jnp.where((donor == order[0]) | (sink == order[0]) | (lengths[sink] == 0), 0, jnp.maximum(room, 0))
    passed = jax.random.randint(jax.random.fold_in(own, 4), (count // 2,), 0, 1 << 20) % (room + 1)
    lengths = lengths.at[donor].add(-passed).at[sink].add(passed)
    items = jnp.searchsorted(jnp.cumsum(lengths), jnp.arange(rows * top), side="right").astype(jnp.int32)
    grid = items.reshape(top, rows).T
    grid = grid[jax.random.permutation(jax.random.fold_in(own, 1), rows)]
    turn = jax.random.randint(jax.random.fold_in(own, 2), (rows, 1), 0, top)
    return jnp.take_along_axis(grid, (jnp.arange(top)[None, :] + turn) % top, axis=1)


def portions_of(count, total, reach, skew, full):
    weights = [(1 << 20) // math.isqrt(rank ** skew) + 1 for rank in range(1, count + 1)]
    largest = reach if full else min(reach, max(-(-total // count), total * weights[0] // sum(weights)))
    least = 1 if total - largest >= count - 1 else 0
    given, spare = [largest] + [least] * (count - 1), total - largest - least * (count - 1)
    while spare > 0:
        candidates = [i for i in range(1, count) if given[i] < largest] or [i for i in range(1, count) if given[i] < reach]
        pool, remaining = sum([weights[i] for i in candidates]), spare
        for i in candidates:
            extra = min(reach - given[i], max(1, remaining * weights[i] // pool), spare)
            given[i] = given[i] + extra
            spare = spare - extra
    return np.array(given)


def gaussian(rng, dims, spread, reach, pieces=(), kind=jnp.bfloat16):
    result = spread * jax.random.normal(rng, dims, jnp.float32)
    if pieces:
        result = result * block_scale(rng, dims, pieces, -0.22, 0.18)
    return jnp.clip(result, -reach, reach).astype(kind)


def setup_inputs(seed: int = 0) -> dict:
    key_list = jax.random.split(jax.random.key(seed), 10)
    context = gaussian(key_list[0], (TOKENS, D), 1.0, 6.0, ((0, 8), (1, 64)))
    out_proj = draw_out_proj(jax.random.fold_in(key_list[9], 71), 0)
    routes_keys = jax.random.split(jax.random.fold_in(key_list[2], 1), TOKENS // TOK_DEV)
    routes_turns = jax.random.permutation(jax.random.fold_in(key_list[2], 3), TOKENS // TOK_DEV)
    routes = jax.vmap(lambda own, number: routed_block(jax.random.fold_in(key_list[2], 2), own, number, TOK_DEV, EXPERTS, TOP, CAP, 2))(routes_keys, routes_turns).reshape((TOKENS, TOP))
    router_logits = gaussian(key_list[3], (TOKENS, TOP), 2.0, 8.0, ((0, 8),), jnp.float32)
    w_gate = gaussian(key_list[4], (EXPERTS * FF, D), D ** -0.5, 0.125, ((0, 64), (1, 8)))
    w_up = gaussian(key_list[5], (EXPERTS * FF, D), D ** -0.5, 0.125, ((0, 64), (1, 8)))
    w_down = gaussian(key_list[6], (EXPERTS * FF, D), FF ** -0.5, 0.078125, ((0, 64), (1, 8)))
    norm_gain = jnp.clip(1.0 + 0.15 * jax.random.normal(key_list[7], (D,), jnp.float32), 0.25, 1.75)
    request_order = jax.random.permutation(key_list[8], TOKENS).astype(jnp.int32)
    return {"context": context, "out_proj": out_proj, "routes": routes, "router_logits": router_logits, "w_gate": w_gate, "w_up": w_up, "w_down": w_down, "norm_gain": norm_gain, "request_order": request_order}


def reference(context, out_proj, routes, router_logits, w_gate, w_up, w_down, norm_gain, request_order):
    attended = jnp.dot(context, out_proj.T, preferred_element_type=jnp.float32).astype(jnp.bfloat16)
    blocks = routes.reshape(N_EXPERT, TOK_DEV * TOP)
    onehot = (blocks[:, :, None] == jnp.arange(EXPERTS, dtype=jnp.int32)[None, None, :]).astype(jnp.int32)
    earlier = jnp.cumsum(onehot, axis=1) - onehot
    slot_index = lax.optimization_barrier(jnp.sum(earlier * onehot, axis=2))
    block_index = jnp.arange(N_EXPERT, dtype=jnp.int32)[:, None]
    destination = (blocks * (N_EXPERT * CAP) + block_index * CAP + slot_index).reshape(-1).astype(jnp.int32)
    source_rows = jnp.repeat(jnp.arange(TOKENS, dtype=jnp.int32), TOP)
    inbox_rows = jnp.zeros((EXPERTS * N_EXPERT * CAP, D), jnp.bfloat16).at[destination].set(attended[source_rows])
    inbox_rows = inbox_rows.reshape(EXPERTS, N_EXPERT * CAP, D)

    def expert_output(operands):
        rows_in, gate_weight, up_weight, down_weight = operands
        gate_value = jnp.dot(rows_in, gate_weight.T, preferred_element_type=jnp.float32)
        up_value = jnp.dot(rows_in, up_weight.T, preferred_element_type=jnp.float32)
        activated = (jax.nn.silu(gate_value) * up_value).astype(jnp.bfloat16)
        return jnp.dot(activated, down_weight, preferred_element_type=jnp.float32)
    outputs = lax.map(expert_output, (inbox_rows, w_gate.reshape(EXPERTS, FF, D), w_up.reshape(EXPERTS, FF, D), w_down.reshape(EXPERTS, FF, D)))
    picked = outputs.reshape(EXPERTS * N_EXPERT * CAP, D)[destination].reshape(TOKENS, TOP, D)
    weights = 1.0 / (1.0 + jnp.exp(router_logits[:, ::-1] - router_logits))
    combined = attended.astype(jnp.float32) + lax.optimization_barrier(jnp.sum(weights[:, :, None] * picked, axis=1))
    mean_square = lax.optimization_barrier(jnp.mean(combined * combined, axis=1, keepdims=True))
    normed = (combined * norm_gain[None, :] * lax.rsqrt(mean_square + 1e-06)).astype(jnp.bfloat16)
    return normed[request_order]
```

```python
import jax
import jax.numpy as jnp
from jax import lax
from jax.sharding import Mesh, PartitionSpec as P

EXPERTS = 8
CAP = 256


epsilon = 1e-06


def slot_targets(routes, capacity, experts):
    flat_routes = routes.reshape(-1)
    onehot = (flat_routes[:, None] == jnp.arange(experts, dtype=jnp.int32)[None, :]).astype(
        jnp.int32
    )
    earlier = jnp.cumsum(onehot, axis=0) - onehot
    slot_index = jnp.sum(earlier * onehot, axis=1)
    return flat_routes * capacity + slot_index


def shards(
    context, out_proj, routes, router_logits, w_gate, w_up, w_down, norm_gain, request_order
):
    tok_rows = context.shape[0]
    feat_local = context.shape[1]
    model_width = out_proj.shape[1]
    mp_count = lax.axis_size(MP)
    copies = mp_count // EXPERTS
    capacity = CAP
    top_k = routes.shape[1]
    gathered = lax.all_gather(
        lax.all_gather(context, "mz", axis=1, tiled=True), "mx", axis=1, tiled=True
    )
    attended = jnp.einsum(
        "td,cd->tc",
        gathered,
        out_proj,
        preferred_element_type=jnp.float32,
    ).astype(jnp.bfloat16)
    destination = slot_targets(routes, capacity, EXPERTS)
    source_rows = jnp.repeat(jnp.arange(tok_rows, dtype=jnp.int32), top_k)
    slotted = (
        jnp.zeros((EXPERTS * capacity, feat_local), jnp.bfloat16)
        .at[destination]
        .set(attended[source_rows])
    )
    slotted = jnp.repeat(slotted.reshape(EXPERTS, capacity, feat_local), copies, axis=0)
    outgoing = slotted.transpose(1, 0, 2).reshape(capacity, mp_count * feat_local)
    inbox_rows = lax.all_to_all(outgoing, MP, split_axis=1, concat_axis=1, tiled=True)
    gate_next = jnp.einsum(
        "rd,hd->rh",
        inbox_rows,
        lax.all_gather(w_gate, EX, axis=1, tiled=True),
        preferred_element_type=jnp.float32,
    )
    up_next = jnp.einsum(
        "rd,hd->rh",
        inbox_rows,
        lax.all_gather(w_up, EX, axis=1, tiled=True),
        preferred_element_type=jnp.float32,
    )
    activated = (jax.nn.silu(gate_next) * up_next).astype(jnp.bfloat16)
    partial_value = jnp.dot(
        activated,
        lax.all_gather(w_down, EX, axis=1, tiled=True),
        preferred_element_type=jnp.float32,
    )
    returned = lax.all_to_all(
        partial_value.astype(jnp.bfloat16), MP, split_axis=1, concat_axis=0, tiled=True
    )
    expert_out = jnp.sum(
        returned.reshape(EXPERTS, copies, capacity, feat_local).astype(jnp.float32), axis=1
    ).reshape(
        EXPERTS * capacity, feat_local
    )
    picked = expert_out[destination].reshape(tok_rows, top_k, feat_local)
    weights = 1.0 / (1.0 + jnp.exp(router_logits[:, ::-1] - router_logits))
    branch = jnp.sum(picked * weights[:, :, None], axis=1)
    combined = attended.astype(jnp.float32) + branch
    squares = lax.psum(lax.psum(jnp.sum(combined * combined, axis=1), "mz"), "mx")
    normed = (
        combined * norm_gain[None, :] * lax.rsqrt(squares / model_width + epsilon)[:, None]
    ).astype(jnp.bfloat16)
    everyone = lax.all_gather(normed, EX, axis=0, tiled=True)
    return everyone[request_order]


EX = ("ey", "ec")
MP = ("mx", "mz")


def split_mesh(mesh):
    devices = mesh.devices
    n_exp, n_mp = devices.shape
    row = devices[0].reshape(-1)
    try:
        z_count = len({d.coords[2] for d in row})
    except (AttributeError, IndexError, TypeError):
        z_count = n_mp
    return Mesh(
        devices.reshape(1, n_exp, n_mp // z_count, z_count), ("ey", "ec", "mx", "mz")
    )


def solution(mesh):
    fine = split_mesh(mesh)
    placed = (
        P(EX, MP),
        P(MP, None),
        P(EX, None),
        P(EX, None),
        P(MP, EX),
        P(MP, EX),
        P(MP, EX),
        P(MP),
        P(EX),
    )
    return jax.shard_map(
        shards, mesh=fine, in_specs=placed, out_specs=P(EX, MP), check_vma=False
    )
```

```python
import jax
import jax.numpy as jnp
from jax import lax
from jax.sharding import Mesh, PartitionSpec as P

EXPERTS = 8
CAP = 256


epsilon = 1e-06


def slot_targets(routes, capacity, experts):
    flat_routes = routes.reshape(-1)
    onehot = (flat_routes[:, None] == jnp.arange(experts, dtype=jnp.int32)[None, :]).astype(
        jnp.int32
    )
    earlier = jnp.cumsum(onehot, axis=0) - onehot
    slot_index = jnp.sum(earlier * onehot, axis=1)
    return flat_routes * capacity + slot_index


def shards(
    context, out_proj, routes, router_logits, w_gate, w_up, w_down, norm_gain, request_order
):
    tok_rows = context.shape[0]
    feat_local = context.shape[1]
    model_width = out_proj.shape[1]
    mp_count = lax.axis_size(MP)
    copies = mp_count // EXPERTS
    capacity = CAP
    top_k = routes.shape[1]
    gathered = lax.all_gather(
        lax.all_gather(context, "mz", axis=1, tiled=True), "mx", axis=1, tiled=True
    )
    attended = jnp.einsum(
        "td,cd->tc",
        gathered,
        out_proj,
        preferred_element_type=jnp.float32,
    ).astype(jnp.bfloat16)
    destination = slot_targets(routes, capacity, EXPERTS)
    source_rows = jnp.repeat(jnp.arange(tok_rows, dtype=jnp.int32), top_k)
    slotted = (
        jnp.zeros((EXPERTS * capacity, feat_local), jnp.bfloat16)
        .at[destination]
        .set(attended[source_rows])
    )
    slotted = jnp.repeat(slotted.reshape(EXPERTS, capacity, feat_local), copies, axis=0)
    outgoing = slotted.transpose(1, 0, 2).reshape(capacity, mp_count * feat_local)
    inbox_rows = lax.all_to_all(outgoing, MP, split_axis=1, concat_axis=1, tiled=True)
    stacked = lax.all_gather(jnp.stack([w_gate, w_up, w_down]), EX, axis=2, tiled=True)
    gate_next = jnp.einsum(
        "rd,hd->rh",
        inbox_rows,
        stacked[0],
        preferred_element_type=jnp.float32,
    )
    up_next = jnp.einsum(
        "rd,hd->rh",
        inbox_rows,
        stacked[1],
        preferred_element_type=jnp.float32,
    )
    activated = (jax.nn.silu(gate_next) * up_next).astype(jnp.bfloat16)
    partial_value = jnp.dot(
        activated,
        stacked[2],
        preferred_element_type=jnp.float32,
    )
    returned = lax.all_to_all(
        partial_value.astype(jnp.bfloat16), MP, split_axis=1, concat_axis=0, tiled=True
    )
    expert_out = jnp.sum(
        returned.reshape(EXPERTS, copies, capacity, feat_local).astype(jnp.float32), axis=1
    ).reshape(
        EXPERTS * capacity, feat_local
    )
    picked = expert_out[destination].reshape(tok_rows, top_k, feat_local)
    weights = 1.0 / (1.0 + jnp.exp(router_logits[:, ::-1] - router_logits))
    branch = jnp.sum(picked * weights[:, :, None], axis=1)
    combined = attended.astype(jnp.float32) + branch
    squares = lax.psum(lax.psum(jnp.sum(combined * combined, axis=1), "mz"), "mx")
    normed = (
        combined * norm_gain[None, :] * lax.rsqrt(squares / model_width + epsilon)[:, None]
    ).astype(jnp.bfloat16)
    everyone = lax.all_gather(normed, EX, axis=0, tiled=True)
    return everyone[request_order]


EX = ("ey", "ec")
MP = ("mx", "mz")


def split_mesh(mesh):
    devices = mesh.devices
    n_exp, n_mp = devices.shape
    row = devices[0].reshape(-1)
    try:
        z_count = len({d.coords[2] for d in row})
    except (AttributeError, IndexError, TypeError):
        z_count = n_mp
    return Mesh(
        devices.reshape(1, n_exp, n_mp // z_count, z_count), ("ey", "ec", "mx", "mz")
    )


def solution(mesh):
    fine = split_mesh(mesh)
    placed = (
        P(EX, MP),
        P(MP, None),
        P(EX, None),
        P(EX, None),
        P(MP, EX),
        P(MP, EX),
        P(MP, EX),
        P(MP),
        P(EX),
    )
    return jax.shard_map(
        shards, mesh=fine, in_specs=placed, out_specs=P(EX, MP), check_vma=False
    )
```

```python
import jax
import jax.numpy as jnp
from jax import lax
from jax.sharding import Mesh, PartitionSpec as P

EXPERTS = 8
CAP = 256


epsilon = 1e-06


def slot_targets(routes, capacity, experts):
    flat_routes = routes.reshape(-1)
    onehot = (flat_routes[:, None] == jnp.arange(experts, dtype=jnp.int32)[None, :]).astype(
        jnp.int32
    )
    earlier = jnp.cumsum(onehot, axis=0) - onehot
    slot_index = jnp.sum(earlier * onehot, axis=1)
    return flat_routes * capacity + slot_index


def shards(
    context, out_proj, routes, router_logits, w_gate, w_up, w_down, norm_gain, request_order
):
    tok_rows = context.shape[0]
    feat_local = context.shape[1]
    model_width = out_proj.shape[1]
    mp_count = lax.axis_size(MP)
    copies = mp_count // EXPERTS
    capacity = CAP
    top_k = routes.shape[1]
    x_count = lax.axis_size("mx")
    x_at = lax.axis_index("mx")
    along_z = lax.all_gather(context, "mz", axis=1, tiled=True)
    z_width = along_z.shape[1]
    rows_x = lax.all_gather(out_proj, "mx", axis=0, tiled=True)
    rows_x = lax.dynamic_slice_in_dim(rows_x, x_at * z_width, z_width, axis=1)
    partial_attended = jnp.einsum(
        "td,cd->tc", along_z, rows_x, preferred_element_type=jnp.float32
    )
    attended = lax.psum_scatter(
        partial_attended, "mx", scatter_dimension=1, tiled=True
    ).astype(jnp.bfloat16)
    destination = slot_targets(routes, capacity, EXPERTS)
    source_rows = jnp.repeat(jnp.arange(tok_rows, dtype=jnp.int32), top_k)
    slotted = (
        jnp.zeros((EXPERTS * capacity, feat_local), jnp.bfloat16)
        .at[destination]
        .set(attended[source_rows])
    )
    slotted = jnp.repeat(slotted.reshape(EXPERTS, capacity, feat_local), copies, axis=0)
    outgoing = slotted.transpose(1, 0, 2).reshape(capacity, mp_count * feat_local)
    inbox_rows = lax.all_to_all(outgoing, MP, split_axis=1, concat_axis=1, tiled=True)
    stacked = lax.all_gather(jnp.stack([w_gate, w_up, w_down]), EX, axis=2, tiled=True)
    gate_next = jnp.einsum(
        "rd,hd->rh",
        inbox_rows,
        stacked[0],
        preferred_element_type=jnp.float32,
    )
    up_next = jnp.einsum(
        "rd,hd->rh",
        inbox_rows,
        stacked[1],
        preferred_element_type=jnp.float32,
    )
    activated = (jax.nn.silu(gate_next) * up_next).astype(jnp.bfloat16)
    partial_value = jnp.dot(
        activated,
        stacked[2],
        preferred_element_type=jnp.float32,
    )
    returned = lax.all_to_all(
        partial_value.astype(jnp.bfloat16), MP, split_axis=1, concat_axis=0, tiled=True
    )
    expert_out = jnp.sum(
        returned.reshape(EXPERTS, copies, capacity, feat_local).astype(jnp.float32), axis=1
    ).reshape(
        EXPERTS * capacity, feat_local
    )
    picked = expert_out[destination].reshape(tok_rows, top_k, feat_local)
    weights = 1.0 / (1.0 + jnp.exp(router_logits[:, ::-1] - router_logits))
    branch = jnp.sum(picked * weights[:, :, None], axis=1)
    combined = attended.astype(jnp.float32) + branch
    squares = lax.psum(lax.psum(jnp.sum(combined * combined, axis=1), "mz"), "mx")
    normed = (
        combined * norm_gain[None, :] * lax.rsqrt(squares / model_width + epsilon)[:, None]
    ).astype(jnp.bfloat16)
    everyone = lax.all_gather(normed, EX, axis=0, tiled=True)
    return everyone[request_order]


EX = ("ey", "ec")
MP = ("mx", "mz")


def split_mesh(mesh):
    devices = mesh.devices
    n_exp, n_mp = devices.shape
    row = devices[0].reshape(-1)
    try:
        z_count = len({d.coords[2] for d in row})
    except (AttributeError, IndexError, TypeError):
        z_count = n_mp
    return Mesh(
        devices.reshape(1, n_exp, n_mp // z_count, z_count), ("ey", "ec", "mx", "mz")
    )


def solution(mesh):
    fine = split_mesh(mesh)
    placed = (
        P(EX, MP),
        P(MP, None),
        P(EX, None),
        P(EX, None),
        P(MP, EX),
        P(MP, EX),
        P(MP, EX),
        P(MP),
        P(EX),
    )
    return jax.shard_map(
        shards, mesh=fine, in_specs=placed, out_specs=P(EX, MP), check_vma=False
    )
```

```python
import jax
import jax.numpy as jnp
from jax import lax
from jax.sharding import Mesh, PartitionSpec as P

EXPERTS = 8
CAP = 256


epsilon = 1e-06


def slot_targets(routes, capacity, experts):
    flat_routes = routes.reshape(-1)
    onehot = (flat_routes[:, None] == jnp.arange(experts, dtype=jnp.int32)[None, :]).astype(
        jnp.int32
    )
    earlier = jnp.cumsum(onehot, axis=0) - onehot
    slot_index = jnp.sum(earlier * onehot, axis=1)
    return flat_routes * capacity + slot_index


def shards(
    context, out_proj, routes, router_logits, w_gate, w_up, w_down, norm_gain, request_order
):
    tok_rows = context.shape[0]
    feat_local = context.shape[1]
    model_width = out_proj.shape[1]
    mp_count = lax.axis_size(MP)
    copies = mp_count // EXPERTS
    capacity = CAP
    top_k = routes.shape[1]
    x_count = lax.axis_size("mx")
    x_at = lax.axis_index("mx")
    along_z = lax.all_gather(context, "mz", axis=1, tiled=True)
    z_width = along_z.shape[1]
    rows_x = lax.all_gather(out_proj, "mx", axis=0, tiled=True)
    rows_x = lax.dynamic_slice_in_dim(rows_x, x_at * z_width, z_width, axis=1)
    partial_attended = jnp.einsum(
        "td,cd->tc", along_z, rows_x, preferred_element_type=jnp.float32
    )
    attended = jnp.sum(
        lax.all_to_all(
            partial_attended.reshape(tok_rows, x_count, feat_local),
            "mx",
            split_axis=1,
            concat_axis=1,
            tiled=True,
        ),
        axis=1,
    ).astype(jnp.bfloat16)
    destination = slot_targets(routes, capacity, EXPERTS)
    source_rows = jnp.repeat(jnp.arange(tok_rows, dtype=jnp.int32), top_k)
    slotted = (
        jnp.zeros((EXPERTS * capacity, feat_local), jnp.bfloat16)
        .at[destination]
        .set(attended[source_rows])
    )
    slotted = jnp.repeat(slotted.reshape(EXPERTS, capacity, feat_local), copies, axis=0)
    outgoing = slotted.transpose(1, 0, 2).reshape(capacity, mp_count * feat_local)
    inbox_rows = lax.all_to_all(outgoing, MP, split_axis=1, concat_axis=1, tiled=True)
    stacked = lax.all_gather(jnp.stack([w_gate, w_up, w_down]), EX, axis=2, tiled=True)
    gate_next = jnp.einsum(
        "rd,hd->rh",
        inbox_rows,
        stacked[0],
        preferred_element_type=jnp.float32,
    )
    up_next = jnp.einsum(
        "rd,hd->rh",
        inbox_rows,
        stacked[1],
        preferred_element_type=jnp.float32,
    )
    activated = (jax.nn.silu(gate_next) * up_next).astype(jnp.bfloat16)
    partial_value = jnp.dot(
        activated,
        stacked[2],
        preferred_element_type=jnp.float32,
    )
    returned = lax.all_to_all(
        partial_value.astype(jnp.bfloat16), MP, split_axis=1, concat_axis=0, tiled=True
    )
    expert_out = jnp.sum(
        returned.reshape(EXPERTS, copies, capacity, feat_local).astype(jnp.float32), axis=1
    ).reshape(
        EXPERTS * capacity, feat_local
    )
    picked = expert_out[destination].reshape(tok_rows, top_k, feat_local)
    weights = 1.0 / (1.0 + jnp.exp(router_logits[:, ::-1] - router_logits))
    branch = jnp.sum(picked * weights[:, :, None], axis=1)
    combined = attended.astype(jnp.float32) + branch
    squares = jnp.sum(
        lax.all_gather(jnp.sum(combined * combined, axis=1), "mz", axis=0), axis=0
    )
    squares = jnp.sum(lax.all_gather(squares, "mx", axis=0), axis=0)
    normed = (
        combined * norm_gain[None, :] * lax.rsqrt(squares / model_width + epsilon)[:, None]
    ).astype(jnp.bfloat16)
    everyone = lax.all_gather(normed, EX, axis=0, tiled=True)
    return everyone[request_order]


EX = ("ey", "ec")
MP = ("mx", "mz")


def split_mesh(mesh):
    devices = mesh.devices
    n_exp, n_mp = devices.shape
    row = devices[0].reshape(-1)
    try:
        z_count = len({d.coords[2] for d in row})
    except (AttributeError, IndexError, TypeError):
        z_count = n_mp
    return Mesh(
        devices.reshape(1, n_exp, n_mp // z_count, z_count), ("ey", "ec", "mx", "mz")
    )


def solution(mesh):
    fine = split_mesh(mesh)
    placed = (
        P(EX, MP),
        P(MP, None),
        P(EX, None),
        P(EX, None),
        P(MP, EX),
        P(MP, EX),
        P(MP, EX),
        P(MP),
        P(EX),
    )
    return jax.shard_map(
        shards, mesh=fine, in_specs=placed, out_specs=P(EX, MP), check_vma=False
    )
```

```python
import jax
import jax.numpy as jnp
from jax import lax
from jax.sharding import Mesh, PartitionSpec as P

EXPERTS = 8
CAP = 256


epsilon = 1e-06


def slot_targets(routes, capacity, experts):
    flat_routes = routes.reshape(-1)
    onehot = (flat_routes[:, None] == jnp.arange(experts, dtype=jnp.int32)[None, :]).astype(
        jnp.int32
    )
    earlier = jnp.cumsum(onehot, axis=0) - onehot
    slot_index = jnp.sum(earlier * onehot, axis=1)
    return flat_routes * capacity + slot_index


def shards(
    context, out_proj, routes, router_logits, w_gate, w_up, w_down, norm_gain, request_order
):
    tok_rows = context.shape[0]
    feat_local = context.shape[1]
    model_width = out_proj.shape[1]
    mp_count = lax.axis_size(MP)
    copies = mp_count // EXPERTS
    capacity = CAP
    top_k = routes.shape[1]
    x_count = lax.axis_size("mx")
    x_at = lax.axis_index("mx")
    along_z = lax.all_gather(
        lax.all_gather(context, "mzb", axis=1, tiled=True), "mza", axis=1, tiled=True
    )
    z_width = along_z.shape[1]
    rows_x = lax.all_gather(out_proj, "mx", axis=0, tiled=True)
    rows_x = lax.dynamic_slice_in_dim(rows_x, x_at * z_width, z_width, axis=1)
    partial_attended = jnp.einsum(
        "td,cd->tc", along_z, rows_x, preferred_element_type=jnp.float32
    )
    attended = jnp.sum(
        lax.all_to_all(
            partial_attended.reshape(tok_rows, x_count, feat_local),
            "mx",
            split_axis=1,
            concat_axis=1,
            tiled=True,
        ),
        axis=1,
    ).astype(jnp.bfloat16)
    destination = slot_targets(routes, capacity, EXPERTS)
    source_rows = jnp.repeat(jnp.arange(tok_rows, dtype=jnp.int32), top_k)
    slotted = (
        jnp.zeros((EXPERTS * capacity, feat_local), jnp.bfloat16)
        .at[destination]
        .set(attended[source_rows])
    )
    slotted = jnp.repeat(slotted.reshape(EXPERTS, capacity, feat_local), copies, axis=0)
    outgoing = slotted.transpose(1, 0, 2).reshape(capacity, mp_count * feat_local)
    inbox_rows = lax.all_to_all(outgoing, MP, split_axis=1, concat_axis=1, tiled=True)
    stacked = lax.all_gather(jnp.stack([w_gate, w_up, w_down]), EX, axis=2, tiled=True)
    gate_next = jnp.einsum(
        "rd,hd->rh",
        inbox_rows,
        stacked[0],
        preferred_element_type=jnp.float32,
    )
    up_next = jnp.einsum(
        "rd,hd->rh",
        inbox_rows,
        stacked[1],
        preferred_element_type=jnp.float32,
    )
    activated = (jax.nn.silu(gate_next) * up_next).astype(jnp.bfloat16)
    partial_value = jnp.dot(
        activated,
        stacked[2],
        preferred_element_type=jnp.float32,
    )
    returned = lax.all_to_all(
        partial_value.astype(jnp.bfloat16), MP, split_axis=1, concat_axis=0, tiled=True
    )
    expert_out = jnp.sum(
        returned.reshape(EXPERTS, copies, capacity, feat_local).astype(jnp.float32), axis=1
    ).reshape(
        EXPERTS * capacity, feat_local
    )
    picked = expert_out[destination].reshape(tok_rows, top_k, feat_local)
    weights = 1.0 / (1.0 + jnp.exp(router_logits[:, ::-1] - router_logits))
    branch = jnp.sum(picked * weights[:, :, None], axis=1)
    combined = attended.astype(jnp.float32) + branch
    squares = jnp.sum(combined * combined, axis=1)
    squares = jnp.sum(lax.all_gather(squares, "mzb", axis=0), axis=0)
    squares = jnp.sum(lax.all_gather(squares, "mza", axis=0), axis=0)
    squares = jnp.sum(lax.all_gather(squares, "mx", axis=0), axis=0)
    normed = (
        combined * norm_gain[None, :] * lax.rsqrt(squares / model_width + epsilon)[:, None]
    ).astype(jnp.bfloat16)
    everyone = lax.all_gather(normed, EX, axis=0, tiled=True)
    return everyone[request_order]


EX = ("ey", "ec")
MP = ("mx", "mza", "mzb")


def split_mesh(mesh):
    devices = mesh.devices
    n_exp, n_mp = devices.shape
    row = devices[0].reshape(-1)
    try:
        z_count = len({d.coords[2] for d in row})
    except (AttributeError, IndexError, TypeError):
        z_count = n_mp
    z_low = 4 if z_count % 4 == 0 else 1
    return Mesh(
        devices.reshape(1, n_exp, n_mp // z_count, z_count // z_low, z_low),
        ("ey", "ec", "mx", "mza", "mzb"),
    )


def solution(mesh):
    fine = split_mesh(mesh)
    placed = (
        P(EX, MP),
        P(MP, None),
        P(EX, None),
        P(EX, None),
        P(MP, EX),
        P(MP, EX),
        P(MP, EX),
        P(MP),
        P(EX),
    )
    return jax.shard_map(
        shards, mesh=fine, in_specs=placed, out_specs=P(EX, MP), check_vma=False
    )
```

```python
import jax
import jax.numpy as jnp
from jax import lax
from jax.sharding import Mesh, PartitionSpec as P

EXPERTS = 8
CAP = 256


epsilon = 1e-06


def slot_targets(routes, capacity, experts):
    flat_routes = routes.reshape(-1)
    onehot = (flat_routes[:, None] == jnp.arange(experts, dtype=jnp.int32)[None, :]).astype(
        jnp.int32
    )
    earlier = jnp.cumsum(onehot, axis=0) - onehot
    slot_index = jnp.sum(earlier * onehot, axis=1)
    return flat_routes * capacity + slot_index


def shards(
    context, out_proj, routes, router_logits, w_gate, w_up, w_down, norm_gain, request_order
):
    tok_rows = context.shape[0]
    feat_local = context.shape[1]
    model_width = out_proj.shape[1]
    mp_count = lax.axis_size(MP)
    copies = mp_count // EXPERTS
    capacity = CAP
    top_k = routes.shape[1]
    x_count = lax.axis_size("mx")
    x_at = lax.axis_index("mx")
    along_z = lax.all_gather(context, "mz", axis=1, tiled=True)
    z_width = along_z.shape[1]
    rows_x = lax.all_to_all(
        jnp.broadcast_to(out_proj[None], (x_count,) + out_proj.shape),
        "mx",
        split_axis=0,
        concat_axis=0,
        tiled=True,
    ).reshape(x_count * feat_local, model_width)
    rows_x = lax.dynamic_slice_in_dim(rows_x, x_at * z_width, z_width, axis=1)
    partial_attended = jnp.einsum(
        "td,cd->tc", along_z, rows_x, preferred_element_type=jnp.float32
    )
    attended = jnp.sum(
        lax.all_to_all(
            partial_attended.reshape(tok_rows, x_count, feat_local),
            "mx",
            split_axis=1,
            concat_axis=1,
            tiled=True,
        ),
        axis=1,
    ).astype(jnp.bfloat16)
    destination = slot_targets(routes, capacity, EXPERTS)
    source_rows = jnp.repeat(jnp.arange(tok_rows, dtype=jnp.int32), top_k)
    slotted = (
        jnp.zeros((EXPERTS * capacity, feat_local), jnp.bfloat16)
        .at[destination]
        .set(attended[source_rows])
    )
    slotted = jnp.repeat(slotted.reshape(EXPERTS, capacity, feat_local), copies, axis=0)
    outgoing = slotted.transpose(1, 0, 2).reshape(capacity, mp_count * feat_local)
    inbox_rows = lax.all_to_all(outgoing, MP, split_axis=1, concat_axis=1, tiled=True)
    stacked = lax.all_gather(jnp.stack([w_gate, w_up, w_down]), EX, axis=2, tiled=True)
    gate_next = jnp.einsum(
        "rd,hd->rh",
        inbox_rows,
        stacked[0],
        preferred_element_type=jnp.float32,
    )
    up_next = jnp.einsum(
        "rd,hd->rh",
        inbox_rows,
        stacked[1],
        preferred_element_type=jnp.float32,
    )
    activated = (jax.nn.silu(gate_next) * up_next).astype(jnp.bfloat16)
    partial_value = jnp.dot(
        activated,
        stacked[2],
        preferred_element_type=jnp.float32,
    )
    returned = lax.all_to_all(
        partial_value.astype(jnp.bfloat16), MP, split_axis=1, concat_axis=0, tiled=True
    )
    expert_out = jnp.sum(
        returned.reshape(EXPERTS, copies, capacity, feat_local).astype(jnp.float32), axis=1
    ).reshape(
        EXPERTS * capacity, feat_local
    )
    picked = expert_out[destination].reshape(tok_rows, top_k, feat_local)
    weights = 1.0 / (1.0 + jnp.exp(router_logits[:, ::-1] - router_logits))
    branch = jnp.sum(picked * weights[:, :, None], axis=1)
    combined = attended.astype(jnp.float32) + branch
    squares = jnp.sum(
        lax.all_gather(jnp.sum(combined * combined, axis=1), "mz", axis=0), axis=0
    )
    squares = jnp.sum(lax.all_gather(squares, "mx", axis=0), axis=0)
    normed = (
        combined * norm_gain[None, :] * lax.rsqrt(squares / model_width + epsilon)[:, None]
    ).astype(jnp.bfloat16)
    everyone = lax.all_gather(normed, EX, axis=0, tiled=True)
    return everyone[request_order]


EX = ("ey", "ec")
MP = ("mx", "mz")


def split_mesh(mesh):
    devices = mesh.devices
    n_exp, n_mp = devices.shape
    row = devices[0].reshape(-1)
    try:
        z_count = len({d.coords[2] for d in row})
    except (AttributeError, IndexError, TypeError):
        z_count = n_mp
    return Mesh(
        devices.reshape(1, n_exp, n_mp // z_count, z_count), ("ey", "ec", "mx", "mz")
    )


def solution(mesh):
    fine = split_mesh(mesh)
    placed = (
        P(EX, MP),
        P(MP, None),
        P(EX, None),
        P(EX, None),
        P(MP, EX),
        P(MP, EX),
        P(MP, EX),
        P(MP),
        P(EX),
    )
    return jax.shard_map(
        shards, mesh=fine, in_specs=placed, out_specs=P(EX, MP), check_vma=False
    )
```

```python
import jax
import jax.numpy as jnp
from jax import lax
from jax.sharding import Mesh, PartitionSpec as P

EXPERTS = 8
CAP = 256


epsilon = 1e-06


def slot_targets(routes, capacity, experts):
    flat_routes = routes.reshape(-1)
    onehot = (flat_routes[:, None] == jnp.arange(experts, dtype=jnp.int32)[None, :]).astype(
        jnp.int32
    )
    earlier = jnp.cumsum(onehot, axis=0) - onehot
    slot_index = jnp.sum(earlier * onehot, axis=1)
    return flat_routes * capacity + slot_index


def shards(
    context, out_proj, routes, router_logits, w_gate, w_up, w_down, norm_gain, request_order
):
    tok_rows = context.shape[0]
    feat_local = context.shape[1]
    model_width = out_proj.shape[1]
    mp_count = lax.axis_size(MP)
    copies = mp_count // EXPERTS
    capacity = CAP
    top_k = routes.shape[1]
    x_count = lax.axis_size("mx")
    x_at = lax.axis_index("mx")
    along_z = lax.all_gather(context, MZ, axis=1, tiled=True)
    z_width = along_z.shape[1]
    rows_x = lax.all_to_all(
        jnp.broadcast_to(out_proj[None], (x_count,) + out_proj.shape),
        "mx",
        split_axis=0,
        concat_axis=0,
        tiled=True,
    ).reshape(x_count * feat_local, model_width)
    rows_x = lax.dynamic_slice_in_dim(rows_x, x_at * z_width, z_width, axis=1)
    partial_attended = jnp.einsum(
        "td,cd->tc", along_z, rows_x, preferred_element_type=jnp.float32
    )
    attended = jnp.sum(
        lax.all_to_all(
            partial_attended.reshape(tok_rows, x_count, feat_local),
            "mx",
            split_axis=1,
            concat_axis=1,
            tiled=True,
        ),
        axis=1,
    ).astype(jnp.bfloat16)
    destination = slot_targets(routes, capacity, EXPERTS)
    source_rows = jnp.repeat(jnp.arange(tok_rows, dtype=jnp.int32), top_k)
    slotted = (
        jnp.zeros((EXPERTS * capacity, feat_local), jnp.bfloat16)
        .at[destination]
        .set(attended[source_rows])
    )
    one_copy = lax.all_to_all(
        slotted.reshape(EXPERTS, capacity, feat_local),
        ("mx", "mzh"),
        split_axis=0,
        concat_axis=0,
        tiled=True,
    )
    inbox_rows = (
        lax.all_gather(one_copy, "mzl", axis=0)
        .transpose(2, 1, 0, 3)
        .reshape(capacity, mp_count * feat_local)
    )
    stacked = lax.all_gather(jnp.stack([w_gate, w_up, w_down]), EX, axis=2, tiled=True)
    gate_next = jnp.einsum(
        "rd,hd->rh",
        inbox_rows,
        stacked[0],
        preferred_element_type=jnp.float32,
    )
    up_next = jnp.einsum(
        "rd,hd->rh",
        inbox_rows,
        stacked[1],
        preferred_element_type=jnp.float32,
    )
    activated = (jax.nn.silu(gate_next) * up_next).astype(jnp.bfloat16)
    partial_value = jnp.dot(
        activated,
        stacked[2],
        preferred_element_type=jnp.float32,
    )
    returned = lax.all_to_all(
        partial_value.astype(jnp.bfloat16), MP, split_axis=1, concat_axis=0, tiled=True
    )
    expert_out = jnp.sum(
        returned.reshape(EXPERTS, copies, capacity, feat_local).astype(jnp.float32), axis=1
    ).reshape(
        EXPERTS * capacity, feat_local
    )
    picked = expert_out[destination].reshape(tok_rows, top_k, feat_local)
    weights = 1.0 / (1.0 + jnp.exp(router_logits[:, ::-1] - router_logits))
    branch = jnp.sum(picked * weights[:, :, None], axis=1)
    combined = attended.astype(jnp.float32) + branch
    squares = jnp.sum(
        lax.all_gather(jnp.sum(combined * combined, axis=1), MZ, axis=0), axis=0
    )
    squares = jnp.sum(lax.all_gather(squares, "mx", axis=0), axis=0)
    normed = (
        combined * norm_gain[None, :] * lax.rsqrt(squares / model_width + epsilon)[:, None]
    ).astype(jnp.bfloat16)
    everyone = lax.all_gather(normed, EX, axis=0, tiled=True)
    return everyone[request_order]


EX = ("ey", "ec")
MZ = ("mzh", "mzl")
MP = ("mx",) + MZ


def split_mesh(mesh):
    devices = mesh.devices
    n_exp, n_mp = devices.shape
    row = devices[0].reshape(-1)
    try:
        z_count = len({d.coords[2] for d in row})
    except (AttributeError, IndexError, TypeError):
        z_count = n_mp
    group = n_mp // EXPERTS
    return Mesh(
        devices.reshape(1, n_exp, n_mp // z_count, z_count // group, group),
        ("ey", "ec", "mx", "mzh", "mzl"),
    )


def solution(mesh):
    fine = split_mesh(mesh)
    placed = (
        P(EX, MP),
        P(MP, None),
        P(EX, None),
        P(EX, None),
        P(MP, EX),
        P(MP, EX),
        P(MP, EX),
        P(MP),
        P(EX),
    )
    return jax.shard_map(
        shards, mesh=fine, in_specs=placed, out_specs=P(EX, MP), check_vma=False
    )
```

```python
import jax
import jax.numpy as jnp
from jax import lax
from jax.sharding import Mesh, PartitionSpec as P

EXPERTS = 8
CAP = 256


epsilon = 1e-06


def slot_targets(routes, capacity, experts):
    flat_routes = routes.reshape(-1)
    onehot = (flat_routes[:, None] == jnp.arange(experts, dtype=jnp.int32)[None, :]).astype(
        jnp.int32
    )
    earlier = jnp.cumsum(onehot, axis=0) - onehot
    slot_index = jnp.sum(earlier * onehot, axis=1)
    return flat_routes * capacity + slot_index


def shards(
    context, out_proj, routes, router_logits, w_gate, w_up, w_down, norm_gain, request_order
):
    tok_rows = context.shape[0]
    feat_local = context.shape[1]
    model_width = out_proj.shape[1]
    mp_count = lax.axis_size(MP)
    copies = mp_count // EXPERTS
    capacity = CAP
    top_k = routes.shape[1]
    x_count = lax.axis_size("mx")
    x_at = lax.axis_index("mx")
    along_z = lax.all_gather(context, "mz", axis=1, tiled=True)
    z_width = along_z.shape[1]
    rows_x = lax.all_to_all(
        jnp.broadcast_to(out_proj[None], (x_count,) + out_proj.shape),
        "mx",
        split_axis=0,
        concat_axis=0,
        tiled=True,
    ).reshape(x_count * feat_local, model_width)
    rows_x = lax.dynamic_slice_in_dim(rows_x, x_at * z_width, z_width, axis=1)
    partial_attended = jnp.einsum(
        "td,cd->tc", along_z, rows_x, preferred_element_type=jnp.float32
    )
    attended = jnp.sum(
        lax.all_to_all(
            partial_attended.reshape(tok_rows, x_count, feat_local),
            "mx",
            split_axis=1,
            concat_axis=1,
            tiled=True,
        ),
        axis=1,
    ).astype(jnp.bfloat16)
    destination = slot_targets(routes, capacity, EXPERTS)
    slot_ids = jnp.arange(EXPERTS * capacity, dtype=jnp.int32)
    chosen = destination.reshape(tok_rows, top_k)[None, :, :] == slot_ids[:, None, None]
    placing = jnp.any(chosen, axis=2).astype(jnp.bfloat16)
    slotted = jnp.dot(placing, attended, preferred_element_type=jnp.float32).astype(
        jnp.bfloat16
    )
    slotted = jnp.repeat(slotted.reshape(EXPERTS, capacity, feat_local), copies, axis=0)
    outgoing = slotted.transpose(1, 0, 2).reshape(capacity, mp_count * feat_local)
    inbox_rows = lax.all_to_all(outgoing, MP, split_axis=1, concat_axis=1, tiled=True)
    stacked = lax.all_gather(jnp.stack([w_gate, w_up, w_down]), EX, axis=2, tiled=True)
    gate_next = jnp.einsum(
        "rd,hd->rh",
        inbox_rows,
        stacked[0],
        preferred_element_type=jnp.float32,
    )
    up_next = jnp.einsum(
        "rd,hd->rh",
        inbox_rows,
        stacked[1],
        preferred_element_type=jnp.float32,
    )
    activated = (jax.nn.silu(gate_next) * up_next).astype(jnp.bfloat16)
    partial_value = jnp.dot(
        activated,
        stacked[2],
        preferred_element_type=jnp.float32,
    )
    returned = lax.all_to_all(
        partial_value.astype(jnp.bfloat16), MP, split_axis=1, concat_axis=0, tiled=True
    )
    expert_out = jnp.sum(
        returned.reshape(EXPERTS, copies, capacity, feat_local).astype(jnp.float32), axis=1
    ).reshape(
        EXPERTS * capacity, feat_local
    )
    weights = 1.0 / (1.0 + jnp.exp(router_logits[:, ::-1] - router_logits))
    picking = jnp.sum(
        jnp.where(chosen, weights[None, :, :], 0.0), axis=2
    ).T
    branch = jnp.dot(
        picking, expert_out, precision=lax.Precision.HIGHEST, preferred_element_type=jnp.float32
    )
    combined = attended.astype(jnp.float32) + branch
    squares = jnp.sum(
        lax.all_gather(jnp.sum(combined * combined, axis=1), "mz", axis=0), axis=0
    )
    squares = jnp.sum(lax.all_gather(squares, "mx", axis=0), axis=0)
    normed = (
        combined * norm_gain[None, :] * lax.rsqrt(squares / model_width + epsilon)[:, None]
    ).astype(jnp.bfloat16)
    everyone = lax.all_gather(normed, EX, axis=0, tiled=True)
    return everyone[request_order]


EX = ("ey", "ec")
MP = ("mx", "mz")


def split_mesh(mesh):
    devices = mesh.devices
    n_exp, n_mp = devices.shape
    row = devices[0].reshape(-1)
    try:
        z_count = len({d.coords[2] for d in row})
    except (AttributeError, IndexError, TypeError):
        z_count = n_mp
    return Mesh(
        devices.reshape(1, n_exp, n_mp // z_count, z_count), ("ey", "ec", "mx", "mz")
    )


def solution(mesh):
    fine = split_mesh(mesh)
    placed = (
        P(EX, MP),
        P(MP, None),
        P(EX, None),
        P(EX, None),
        P(MP, EX),
        P(MP, EX),
        P(MP, EX),
        P(MP),
        P(EX),
    )
    return jax.shard_map(
        shards, mesh=fine, in_specs=placed, out_specs=P(EX, MP), check_vma=False
    )
```

```python
import jax
import jax.numpy as jnp
from jax import lax
from jax.sharding import Mesh, PartitionSpec as P

EXPERTS = 8
CAP = 256


epsilon = 1e-06


def slot_targets(routes, capacity, experts):
    flat_routes = routes.reshape(-1)
    onehot = (flat_routes[:, None] == jnp.arange(experts, dtype=jnp.int32)[None, :]).astype(
        jnp.int32
    )
    earlier = jnp.cumsum(onehot, axis=0) - onehot
    slot_index = jnp.sum(earlier * onehot, axis=1)
    return flat_routes * capacity + slot_index


def gather_sum(values, axis):
    count = lax.axis_size(axis)
    spread = jnp.broadcast_to(values[None], (count,) + values.shape)
    return jnp.sum(lax.all_to_all(spread, axis, 0, 0, tiled=True), axis=0)


def shards(
    context, out_proj, routes, router_logits, w_gate, w_up, w_down, norm_gain, request_order
):
    tok_rows = context.shape[0]
    feat_local = context.shape[1]
    model_width = out_proj.shape[1]
    mp_count = lax.axis_size(MP)
    copies = mp_count // EXPERTS
    capacity = CAP
    top_k = routes.shape[1]
    x_count = lax.axis_size("mx")
    x_at = lax.axis_index("mx")
    along_z = lax.all_gather(context, "mz", axis=1, tiled=True)
    z_width = along_z.shape[1]
    rows_x = lax.all_to_all(
        jnp.broadcast_to(out_proj[None], (x_count,) + out_proj.shape),
        "mx",
        split_axis=0,
        concat_axis=0,
        tiled=True,
    ).reshape(x_count * feat_local, model_width)
    rows_x = lax.dynamic_slice_in_dim(rows_x, x_at * z_width, z_width, axis=1)
    partial_attended = jnp.einsum(
        "td,cd->tc", along_z, rows_x, preferred_element_type=jnp.float32
    )
    attended = jnp.sum(
        lax.all_to_all(
            partial_attended.reshape(tok_rows, x_count, feat_local),
            "mx",
            split_axis=1,
            concat_axis=1,
            tiled=True,
        ),
        axis=1,
    ).astype(jnp.bfloat16)
    destination = slot_targets(routes, capacity, EXPERTS)
    slot_ids = jnp.arange(EXPERTS * capacity, dtype=jnp.int32)
    chosen = destination.reshape(tok_rows, top_k)[None, :, :] == slot_ids[:, None, None]
    placing = jnp.any(chosen, axis=2).astype(jnp.bfloat16)
    slotted = jnp.dot(placing, attended, preferred_element_type=jnp.float32).astype(
        jnp.bfloat16
    )
    slotted = jnp.repeat(slotted.reshape(EXPERTS, capacity, feat_local), copies, axis=0)
    outgoing = slotted.transpose(1, 0, 2).reshape(capacity, mp_count * feat_local)
    inbox_rows = lax.all_to_all(outgoing, MP, split_axis=1, concat_axis=1, tiled=True)
    stacked = lax.all_gather(jnp.stack([w_gate, w_up, w_down]), EX, axis=2, tiled=True)
    gate_next = jnp.einsum(
        "rd,hd->rh",
        inbox_rows,
        stacked[0],
        preferred_element_type=jnp.float32,
    )
    up_next = jnp.einsum(
        "rd,hd->rh",
        inbox_rows,
        stacked[1],
        preferred_element_type=jnp.float32,
    )
    activated = (jax.nn.silu(gate_next) * up_next).astype(jnp.bfloat16)
    partial_value = jnp.dot(
        activated,
        stacked[2],
        preferred_element_type=jnp.float32,
    )
    returned = lax.all_to_all(
        partial_value.astype(jnp.bfloat16), MP, split_axis=1, concat_axis=0, tiled=True
    )
    expert_out = jnp.sum(
        returned.reshape(EXPERTS, copies, capacity, feat_local).astype(jnp.float32), axis=1
    ).reshape(
        EXPERTS * capacity, feat_local
    )
    weights = 1.0 / (1.0 + jnp.exp(router_logits[:, ::-1] - router_logits))
    picking = jnp.sum(
        jnp.where(chosen, weights[None, :, :], 0.0), axis=2
    ).T
    branch = jnp.dot(
        picking, expert_out, precision=lax.Precision.HIGHEST, preferred_element_type=jnp.float32
    )
    combined = attended.astype(jnp.float32) + branch
    squares = jnp.sum(combined * combined, axis=1)
    squares = gather_sum(squares, "mz")
    squares = gather_sum(squares, "mx")
    normed = (
        combined * norm_gain[None, :] * lax.rsqrt(squares / model_width + epsilon)[:, None]
    ).astype(jnp.bfloat16)
    everyone = lax.all_gather(normed, EX, axis=0, tiled=True)
    return everyone[request_order]


EX = ("ey", "ec")
MP = ("mx", "mz")


def split_mesh(mesh):
    devices = mesh.devices
    n_exp, n_mp = devices.shape
    row = devices[0].reshape(-1)
    try:
        z_count = len({d.coords[2] for d in row})
    except (AttributeError, IndexError, TypeError):
        z_count = n_mp
    return Mesh(
        devices.reshape(1, n_exp, n_mp // z_count, z_count), ("ey", "ec", "mx", "mz")
    )


def solution(mesh):
    fine = split_mesh(mesh)
    placed = (
        P(EX, MP),
        P(MP, None),
        P(EX, None),
        P(EX, None),
        P(MP, EX),
        P(MP, EX),
        P(MP, EX),
        P(MP),
        P(EX),
    )
    return jax.shard_map(
        shards, mesh=fine, in_specs=placed, out_specs=P(EX, MP), check_vma=False
    )
```

```python
import jax
import jax.numpy as jnp
from jax import lax
from jax.sharding import Mesh, PartitionSpec as P

EXPERTS = 8
CAP = 256


epsilon = 1e-06


def slot_targets(routes, capacity, experts):
    flat_routes = routes.reshape(-1)
    onehot = (flat_routes[:, None] == jnp.arange(experts, dtype=jnp.int32)[None, :]).astype(
        jnp.int32
    )
    earlier = jnp.cumsum(onehot, axis=0) - onehot
    slot_index = jnp.sum(earlier * onehot, axis=1)
    return flat_routes * capacity + slot_index


def gather_sum(values, axis):
    count = lax.axis_size(axis)
    spread = jnp.broadcast_to(values[None], (count,) + values.shape)
    return jnp.sum(lax.all_to_all(spread, axis, 0, 0, tiled=True), axis=0)


def shards(
    context, out_proj, routes, router_logits, w_gate, w_up, w_down, norm_gain, request_order
):
    tok_rows = context.shape[0]
    feat_local = context.shape[1]
    model_width = out_proj.shape[1]
    mp_count = lax.axis_size(MP)
    copies = mp_count // EXPERTS
    capacity = CAP
    top_k = routes.shape[1]
    x_count = lax.axis_size("mx")
    x_at = lax.axis_index("mx")
    z_count = lax.axis_size("mz")
    along_z = lax.all_to_all(
        jnp.broadcast_to(context[None], (z_count,) + context.shape),
        "mz",
        split_axis=0,
        concat_axis=0,
        tiled=True,
    )
    along_z = along_z.transpose(1, 0, 2).reshape(tok_rows, z_count * feat_local)
    z_width = along_z.shape[1]
    rows_x = lax.all_to_all(
        jnp.broadcast_to(out_proj[None], (x_count,) + out_proj.shape),
        "mx",
        split_axis=0,
        concat_axis=0,
        tiled=True,
    ).reshape(x_count * feat_local, model_width)
    rows_x = lax.dynamic_slice_in_dim(rows_x, x_at * z_width, z_width, axis=1)
    partial_attended = jnp.einsum(
        "td,cd->tc", along_z, rows_x, preferred_element_type=jnp.float32
    )
    attended = jnp.sum(
        lax.all_to_all(
            partial_attended.reshape(tok_rows, x_count, feat_local),
            "mx",
            split_axis=1,
            concat_axis=1,
            tiled=True,
        ),
        axis=1,
    ).astype(jnp.bfloat16)
    destination = slot_targets(routes, capacity, EXPERTS)
    slot_ids = jnp.arange(EXPERTS * capacity, dtype=jnp.int32)
    chosen = destination.reshape(tok_rows, top_k)[None, :, :] == slot_ids[:, None, None]
    placing = jnp.any(chosen, axis=2).astype(jnp.bfloat16)
    slotted = jnp.dot(placing, attended, preferred_element_type=jnp.float32).astype(
        jnp.bfloat16
    )
    slotted = jnp.repeat(slotted.reshape(EXPERTS, capacity, feat_local), copies, axis=0)
    outgoing = slotted.transpose(1, 0, 2).reshape(capacity, mp_count * feat_local)
    inbox_rows = lax.all_to_all(outgoing, MP, split_axis=1, concat_axis=1, tiled=True)
    stacked = lax.all_gather(jnp.stack([w_gate, w_up, w_down]), EX, axis=2, tiled=True)
    gate_next = jnp.einsum(
        "rd,hd->rh",
        inbox_rows,
        stacked[0],
        preferred_element_type=jnp.float32,
    )
    up_next = jnp.einsum(
        "rd,hd->rh",
        inbox_rows,
        stacked[1],
        preferred_element_type=jnp.float32,
    )
    activated = (jax.nn.silu(gate_next) * up_next).astype(jnp.bfloat16)
    partial_value = jnp.dot(
        activated,
        stacked[2],
        preferred_element_type=jnp.float32,
    )
    returned = lax.all_to_all(
        partial_value.astype(jnp.bfloat16), MP, split_axis=1, concat_axis=0, tiled=True
    )
    expert_out = jnp.sum(
        returned.reshape(EXPERTS, copies, capacity, feat_local).astype(jnp.float32), axis=1
    ).reshape(
        EXPERTS * capacity, feat_local
    )
    weights = 1.0 / (1.0 + jnp.exp(router_logits[:, ::-1] - router_logits))
    picking = jnp.sum(
        jnp.where(chosen, weights[None, :, :], 0.0), axis=2
    ).T
    branch = jnp.dot(
        picking, expert_out, precision=lax.Precision.HIGHEST, preferred_element_type=jnp.float32
    )
    combined = attended.astype(jnp.float32) + branch
    squares = jnp.sum(combined * combined, axis=1)
    squares = gather_sum(squares, "mz")
    squares = gather_sum(squares, "mx")
    normed = (
        combined * norm_gain[None, :] * lax.rsqrt(squares / model_width + epsilon)[:, None]
    ).astype(jnp.bfloat16)
    ex_count = lax.axis_size(EX)
    everyone = lax.all_to_all(
        jnp.broadcast_to(normed[None], (ex_count,) + normed.shape),
        EX,
        split_axis=0,
        concat_axis=0,
        tiled=True,
    ).reshape(ex_count * tok_rows, feat_local)
    return everyone[request_order]


EX = ("ey", "ec")
MP = ("mx", "mz")


def split_mesh(mesh):
    devices = mesh.devices
    n_exp, n_mp = devices.shape
    row = devices[0].reshape(-1)
    try:
        z_count = len({d.coords[2] for d in row})
    except (AttributeError, IndexError, TypeError):
        z_count = n_mp
    return Mesh(
        devices.reshape(1, n_exp, n_mp // z_count, z_count), ("ey", "ec", "mx", "mz")
    )


def solution(mesh):
    fine = split_mesh(mesh)
    placed = (
        P(EX, MP),
        P(MP, None),
        P(EX, None),
        P(EX, None),
        P(MP, EX),
        P(MP, EX),
        P(MP, EX),
        P(MP),
        P(EX),
    )
    return jax.shard_map(
        shards, mesh=fine, in_specs=placed, out_specs=P(EX, MP), check_vma=False
    )
```

```python
import jax
import jax.numpy as jnp
from jax import lax
from jax.sharding import Mesh, PartitionSpec as P

EXPERTS = 8
CAP = 256


epsilon = 1e-06


def slot_targets(routes, capacity, experts):
    flat_routes = routes.reshape(-1)
    onehot = (flat_routes[:, None] == jnp.arange(experts, dtype=jnp.int32)[None, :]).astype(
        jnp.int32
    )
    earlier = jnp.cumsum(onehot, axis=0) - onehot
    slot_index = jnp.sum(earlier * onehot, axis=1)
    return flat_routes * capacity + slot_index


def gather_sum(values, axis):
    count = lax.axis_size(axis)
    spread = jnp.broadcast_to(values[None], (count,) + values.shape)
    return jnp.sum(lax.all_to_all(spread, axis, 0, 0, tiled=True), axis=0)


def shards(
    context, out_proj, routes, router_logits, w_gate, w_up, w_down, norm_gain, request_order
):
    tok_rows = context.shape[0]
    feat_local = context.shape[1]
    model_width = out_proj.shape[1]
    mp_count = lax.axis_size(MP)
    copies = mp_count // EXPERTS
    capacity = CAP
    top_k = routes.shape[1]
    x_count = lax.axis_size("mx")
    x_at = lax.axis_index("mx")
    along_z = lax.all_gather(context, "mz", axis=1, tiled=True)
    z_width = along_z.shape[1]
    rows_x = lax.all_to_all(
        jnp.broadcast_to(out_proj[None], (x_count,) + out_proj.shape),
        "mx",
        split_axis=0,
        concat_axis=0,
        tiled=True,
    ).reshape(x_count * feat_local, model_width)
    rows_x = lax.dynamic_slice_in_dim(rows_x, x_at * z_width, z_width, axis=1)
    partial_attended = jnp.einsum(
        "td,cd->tc", along_z, rows_x, preferred_element_type=jnp.float32
    )
    attended = jnp.sum(
        lax.all_to_all(
            partial_attended.reshape(tok_rows, x_count, feat_local),
            "mx",
            split_axis=1,
            concat_axis=1,
            tiled=True,
        ),
        axis=1,
    ).astype(jnp.bfloat16)
    destination = slot_targets(routes, capacity, EXPERTS)
    slot_ids = jnp.arange(EXPERTS * capacity, dtype=jnp.int32)
    chosen = destination.reshape(tok_rows, top_k)[None, :, :] == slot_ids[:, None, None]
    placing = jnp.any(chosen, axis=2).astype(jnp.bfloat16)
    slotted = jnp.dot(placing, attended, preferred_element_type=jnp.float32).astype(
        jnp.bfloat16
    )
    slotted = jnp.repeat(slotted.reshape(EXPERTS, capacity, feat_local), copies, axis=0)
    outgoing = slotted.transpose(1, 0, 2).reshape(capacity, mp_count * feat_local)
    inbox_rows = lax.all_to_all(outgoing, MP, split_axis=1, concat_axis=1, tiled=True)
    stacked = lax.all_gather(jnp.stack([w_gate, w_up, w_down]), EX, axis=2, tiled=True)
    gate_next = jnp.einsum(
        "rd,hd->rh",
        inbox_rows,
        stacked[0],
        preferred_element_type=jnp.float32,
    )
    up_next = jnp.einsum(
        "rd,hd->rh",
        inbox_rows,
        stacked[1],
        preferred_element_type=jnp.float32,
    )
    activated = (jax.nn.silu(gate_next) * up_next).astype(jnp.bfloat16)
    partial_value = jnp.dot(
        activated,
        stacked[2],
        preferred_element_type=jnp.float32,
    )
    returned = lax.all_to_all(
        partial_value.astype(jnp.bfloat16), MP, split_axis=1, concat_axis=0, tiled=True
    )
    expert_out = jnp.sum(
        returned.reshape(EXPERTS, copies, capacity, feat_local).astype(jnp.float32), axis=1
    ).reshape(
        EXPERTS * capacity, feat_local
    )
    weights = 1.0 / (1.0 + jnp.exp(router_logits[:, ::-1] - router_logits))
    picking = jnp.sum(
        jnp.where(chosen, weights[None, :, :], 0.0), axis=2
    ).T
    branch = jnp.dot(
        picking, expert_out, precision=lax.Precision.HIGHEST, preferred_element_type=jnp.float32
    )
    combined = attended.astype(jnp.float32) + branch
    squares = jnp.sum(combined * combined, axis=1)
    squares = gather_sum(squares, "mz")
    squares = gather_sum(squares, "mx")
    normed = (
        combined * norm_gain[None, :] * lax.rsqrt(squares / model_width + epsilon)[:, None]
    ).astype(jnp.bfloat16)
    ex_count = lax.axis_size(EX)
    everyone = lax.all_to_all(
        jnp.broadcast_to(normed[None], (ex_count,) + normed.shape),
        EX,
        split_axis=0,
        concat_axis=0,
        tiled=True,
    ).reshape(ex_count * tok_rows, feat_local)
    return everyone[request_order]


EX = ("ey", "ec")
MP = ("mx", "mz")


def split_mesh(mesh):
    devices = mesh.devices
    n_exp, n_mp = devices.shape
    row = devices[0].reshape(-1)
    try:
        z_count = len({d.coords[2] for d in row})
    except (AttributeError, IndexError, TypeError):
        z_count = n_mp
    return Mesh(
        devices.reshape(1, n_exp, n_mp // z_count, z_count), ("ey", "ec", "mx", "mz")
    )


def solution(mesh):
    fine = split_mesh(mesh)
    placed = (
        P(EX, MP),
        P(MP, None),
        P(EX, None),
        P(EX, None),
        P(MP, EX),
        P(MP, EX),
        P(MP, EX),
        P(MP),
        P(EX),
    )
    return jax.shard_map(
        shards, mesh=fine, in_specs=placed, out_specs=P(EX, MP), check_vma=False
    )
```

```python
import jax
import jax.numpy as jnp
from jax import lax
from jax.sharding import Mesh, PartitionSpec as P

EXPERTS = 8
CAP = 256


epsilon = 1e-06


def slot_targets(routes, capacity, experts):
    flat_routes = routes.reshape(-1)
    onehot = (flat_routes[:, None] == jnp.arange(experts, dtype=jnp.int32)[None, :]).astype(
        jnp.int32
    )
    earlier = jnp.cumsum(onehot, axis=0) - onehot
    slot_index = jnp.sum(earlier * onehot, axis=1)
    return flat_routes * capacity + slot_index


def gather_sum(values, axis):
    count = lax.axis_size(axis)
    spread = jnp.broadcast_to(values[None], (count,) + values.shape)
    return jnp.sum(lax.all_to_all(spread, axis, 0, 0, tiled=True), axis=0)


def shards(
    context, out_proj, routes, router_logits, w_gate, w_up, w_down, norm_gain, request_order
):
    tok_rows = context.shape[0]
    feat_local = context.shape[1]
    model_width = out_proj.shape[1]
    mp_count = lax.axis_size(MP)
    copies = mp_count // EXPERTS
    capacity = CAP
    top_k = routes.shape[1]
    x_count = lax.axis_size("mx")
    x_at = lax.axis_index("mx")
    along_z = lax.all_gather(context, "mz", axis=1, tiled=True)
    z_width = along_z.shape[1]
    rows_x = lax.all_to_all(
        jnp.broadcast_to(out_proj[None], (x_count,) + out_proj.shape),
        "mx",
        split_axis=0,
        concat_axis=0,
        tiled=True,
    ).reshape(x_count * feat_local, model_width)
    rows_x = lax.dynamic_slice_in_dim(rows_x, x_at * z_width, z_width, axis=1)
    partial_attended = jnp.einsum(
        "td,cd->tc", along_z, rows_x, preferred_element_type=jnp.float32
    )
    attended = jnp.sum(
        lax.all_to_all(
            partial_attended.reshape(tok_rows, x_count, feat_local),
            "mx",
            split_axis=1,
            concat_axis=1,
            tiled=True,
        ),
        axis=1,
    ).astype(jnp.bfloat16)
    destination = slot_targets(routes, capacity, EXPERTS)
    slot_ids = jnp.arange(EXPERTS * capacity, dtype=jnp.int32)
    chosen = destination.reshape(tok_rows, top_k)[None, :, :] == slot_ids[:, None, None]
    placing = jnp.any(chosen, axis=2).astype(jnp.bfloat16)
    slotted = jnp.dot(placing, attended, preferred_element_type=jnp.float32).astype(
        jnp.bfloat16
    )
    slotted = jnp.repeat(slotted.reshape(EXPERTS, capacity, feat_local), copies, axis=0)
    outgoing = slotted.transpose(1, 0, 2).reshape(capacity, mp_count * feat_local)
    inbox_rows = lax.all_to_all(outgoing, MP, split_axis=1, concat_axis=1, tiled=True)
    stacked = lax.all_gather(jnp.stack([w_gate, w_up, w_down]), EX, axis=2, tiled=True)
    gate_next = jnp.einsum(
        "rd,hd->rh",
        inbox_rows,
        stacked[0],
        preferred_element_type=jnp.float32,
    )
    up_next = jnp.einsum(
        "rd,hd->rh",
        inbox_rows,
        stacked[1],
        preferred_element_type=jnp.float32,
    )
    activated = (jax.nn.silu(gate_next) * up_next).astype(jnp.bfloat16)
    partial_value = jnp.dot(
        activated,
        stacked[2],
        preferred_element_type=jnp.float32,
    )
    returned = lax.all_to_all(
        partial_value.astype(jnp.bfloat16), MP, split_axis=1, concat_axis=0, tiled=True
    )
    expert_out = jnp.sum(
        returned.reshape(EXPERTS, copies, capacity, feat_local).astype(jnp.float32), axis=1
    ).reshape(
        EXPERTS * capacity, feat_local
    )
    weights = 1.0 / (1.0 + jnp.exp(router_logits[:, ::-1] - router_logits))
    picking = jnp.sum(
        jnp.where(chosen, weights[None, :, :], 0.0), axis=2
    ).T
    branch = jnp.dot(
        picking, expert_out, precision=lax.Precision.HIGHEST, preferred_element_type=jnp.float32
    )
    combined = attended.astype(jnp.float32) + branch
    squares = jnp.sum(combined * combined, axis=1)
    squares = gather_sum(squares, MP)
    normed = (
        combined * norm_gain[None, :] * lax.rsqrt(squares / model_width + epsilon)[:, None]
    ).astype(jnp.bfloat16)
    ex_count = lax.axis_size(EX)
    everyone = lax.all_to_all(
        jnp.broadcast_to(normed[None], (ex_count,) + normed.shape),
        EX,
        split_axis=0,
        concat_axis=0,
        tiled=True,
    ).reshape(ex_count * tok_rows, feat_local)
    return everyone[request_order]


EX = ("ey", "ec")
MP = ("mx", "mz")


def split_mesh(mesh):
    devices = mesh.devices
    n_exp, n_mp = devices.shape
    row = devices[0].reshape(-1)
    try:
        z_count = len({d.coords[2] for d in row})
    except (AttributeError, IndexError, TypeError):
        z_count = n_mp
    return Mesh(
        devices.reshape(1, n_exp, n_mp // z_count, z_count), ("ey", "ec", "mx", "mz")
    )


def solution(mesh):
    fine = split_mesh(mesh)
    placed = (
        P(EX, MP),
        P(MP, None),
        P(EX, None),
        P(EX, None),
        P(MP, EX),
        P(MP, EX),
        P(MP, EX),
        P(MP),
        P(EX),
    )
    return jax.shard_map(
        shards, mesh=fine, in_specs=placed, out_specs=P(EX, MP), check_vma=False
    )
```

```python
import jax
import jax.numpy as jnp
from jax import lax
from jax.sharding import Mesh, PartitionSpec as P

EXPERTS = 8
CAP = 256


epsilon = 1e-06


def slot_targets(routes, capacity, experts):
    flat_routes = routes.reshape(-1)
    pairs = flat_routes.shape[0]
    onehot = (flat_routes[:, None] == jnp.arange(experts, dtype=jnp.int32)[None, :]).astype(
        jnp.bfloat16
    )
    order = jnp.arange(pairs, dtype=jnp.int32)
    before = (order[None, :] < order[:, None]).astype(jnp.bfloat16)
    earlier = jnp.dot(before, onehot, preferred_element_type=jnp.float32)
    slot_index = jnp.sum(earlier * onehot.astype(jnp.float32), axis=1).astype(jnp.int32)
    return flat_routes * capacity + slot_index


def gather_sum(values, axis):
    count = lax.axis_size(axis)
    spread = jnp.broadcast_to(values[None], (count,) + values.shape)
    return jnp.sum(lax.all_to_all(spread, axis, 0, 0, tiled=True), axis=0)


def shards(
    context, out_proj, routes, router_logits, w_gate, w_up, w_down, norm_gain, request_order
):
    tok_rows = context.shape[0]
    feat_local = context.shape[1]
    model_width = out_proj.shape[1]
    mp_count = lax.axis_size(MP)
    copies = mp_count // EXPERTS
    capacity = CAP
    top_k = routes.shape[1]
    x_count = lax.axis_size("mx")
    x_at = lax.axis_index("mx")
    along_z = lax.all_gather(context, "mz", axis=1, tiled=True)
    z_width = along_z.shape[1]
    rows_x = lax.all_to_all(
        jnp.broadcast_to(out_proj[None], (x_count,) + out_proj.shape),
        "mx",
        split_axis=0,
        concat_axis=0,
        tiled=True,
    ).reshape(x_count * feat_local, model_width)
    rows_x = lax.dynamic_slice_in_dim(rows_x, x_at * z_width, z_width, axis=1)
    partial_attended = jnp.einsum(
        "td,cd->tc", along_z, rows_x, preferred_element_type=jnp.float32
    )
    attended = jnp.sum(
        lax.all_to_all(
            partial_attended.reshape(tok_rows, x_count, feat_local),
            "mx",
            split_axis=1,
            concat_axis=1,
            tiled=True,
        ),
        axis=1,
    ).astype(jnp.bfloat16)
    destination = slot_targets(routes, capacity, EXPERTS)
    slot_ids = jnp.arange(EXPERTS * capacity, dtype=jnp.int32)
    chosen = destination.reshape(tok_rows, top_k)[None, :, :] == slot_ids[:, None, None]
    placing = jnp.any(chosen, axis=2).astype(jnp.bfloat16)
    slotted = jnp.dot(placing, attended, preferred_element_type=jnp.float32).astype(
        jnp.bfloat16
    )
    slotted = jnp.repeat(slotted.reshape(EXPERTS, capacity, feat_local), copies, axis=0)
    outgoing = slotted.transpose(1, 0, 2).reshape(capacity, mp_count * feat_local)
    inbox_rows = lax.all_to_all(outgoing, MP, split_axis=1, concat_axis=1, tiled=True)
    stacked = lax.all_gather(jnp.stack([w_gate, w_up, w_down]), EX, axis=2, tiled=True)
    gate_next = jnp.einsum(
        "rd,hd->rh",
        inbox_rows,
        stacked[0],
        preferred_element_type=jnp.float32,
    )
    up_next = jnp.einsum(
        "rd,hd->rh",
        inbox_rows,
        stacked[1],
        preferred_element_type=jnp.float32,
    )
    activated = (jax.nn.silu(gate_next) * up_next).astype(jnp.bfloat16)
    partial_value = jnp.dot(
        activated,
        stacked[2],
        preferred_element_type=jnp.float32,
    )
    returned = lax.all_to_all(
        partial_value.astype(jnp.bfloat16), MP, split_axis=1, concat_axis=0, tiled=True
    )
    expert_out = jnp.sum(
        returned.reshape(EXPERTS, copies, capacity, feat_local).astype(jnp.float32), axis=1
    ).reshape(
        EXPERTS * capacity, feat_local
    )
    weights = 1.0 / (1.0 + jnp.exp(router_logits[:, ::-1] - router_logits))
    picking = jnp.sum(
        jnp.where(chosen, weights[None, :, :], 0.0), axis=2
    ).T
    branch = jnp.dot(
        picking, expert_out, precision=lax.Precision.HIGHEST, preferred_element_type=jnp.float32
    )
    combined = attended.astype(jnp.float32) + branch
    squares = jnp.sum(combined * combined, axis=1)
    squares = gather_sum(squares, MP)
    normed = (
        combined * norm_gain[None, :] * lax.rsqrt(squares / model_width + epsilon)[:, None]
    ).astype(jnp.bfloat16)
    ex_count = lax.axis_size(EX)
    everyone = lax.all_to_all(
        jnp.broadcast_to(normed[None], (ex_count,) + normed.shape),
        EX,
        split_axis=0,
        concat_axis=0,
        tiled=True,
    ).reshape(ex_count * tok_rows, feat_local)
    return everyone[request_order]


EX = ("ey", "ec")
MP = ("mx", "mz")


def split_mesh(mesh):
    devices = mesh.devices
    n_exp, n_mp = devices.shape
    row = devices[0].reshape(-1)
    try:
        z_count = len({d.coords[2] for d in row})
    except (AttributeError, IndexError, TypeError):
        z_count = n_mp
    return Mesh(
        devices.reshape(1, n_exp, n_mp // z_count, z_count), ("ey", "ec", "mx", "mz")
    )


def solution(mesh):
    fine = split_mesh(mesh)
    placed = (
        P(EX, MP),
        P(MP, None),
        P(EX, None),
        P(EX, None),
        P(MP, EX),
        P(MP, EX),
        P(MP, EX),
        P(MP),
        P(EX),
    )
    return jax.shard_map(
        shards, mesh=fine, in_specs=placed, out_specs=P(EX, MP), check_vma=False
    )
```

```python
import jax
import jax.numpy as jnp
from jax import lax
from jax.sharding import Mesh, PartitionSpec as P

EXPERTS = 8
CAP = 256


epsilon = 1e-06


def slot_targets(routes, capacity, experts):
    flat_routes = routes.reshape(-1)
    pairs = flat_routes.shape[0]
    onehot = (flat_routes[:, None] == jnp.arange(experts, dtype=jnp.int32)[None, :]).astype(
        jnp.bfloat16
    )
    order = jnp.arange(pairs, dtype=jnp.int32)
    before = (order[None, :] < order[:, None]).astype(jnp.bfloat16)
    earlier = jnp.dot(before, onehot, preferred_element_type=jnp.float32)
    slot_index = jnp.sum(earlier * onehot.astype(jnp.float32), axis=1).astype(jnp.int32)
    return flat_routes * capacity + slot_index


def gather_sum(values, axis):
    count = lax.axis_size(axis)
    spread = jnp.broadcast_to(values[None], (count,) + values.shape)
    return jnp.sum(lax.all_to_all(spread, axis, 0, 0, tiled=True), axis=0)


def shards(
    context, out_proj, routes, router_logits, w_gate, w_up, w_down, norm_gain, request_order
):
    tok_rows = context.shape[0]
    feat_local = context.shape[1]
    model_width = out_proj.shape[1]
    mp_count = lax.axis_size(MP)
    copies = mp_count // EXPERTS
    capacity = CAP
    top_k = routes.shape[1]
    x_count = lax.axis_size("mx")
    x_at = lax.axis_index("mx")
    along_z = lax.all_gather(context, "mz", axis=1, tiled=True)
    z_width = along_z.shape[1]
    rows_x = lax.all_to_all(
        jnp.broadcast_to(out_proj[None], (x_count,) + out_proj.shape),
        "mx",
        split_axis=0,
        concat_axis=0,
        tiled=True,
    ).reshape(x_count * feat_local, model_width)
    rows_x = lax.dynamic_slice_in_dim(rows_x, x_at * z_width, z_width, axis=1)
    partial_attended = jnp.einsum(
        "td,cd->tc", along_z, rows_x, preferred_element_type=jnp.float32
    )
    attended = jnp.sum(
        lax.all_to_all(
            partial_attended.reshape(tok_rows, x_count, feat_local),
            "mx",
            split_axis=1,
            concat_axis=1,
            tiled=True,
        ),
        axis=1,
    ).astype(jnp.bfloat16)
    destination = slot_targets(routes, capacity, EXPERTS)
    slot_ids = jnp.arange(EXPERTS * capacity, dtype=jnp.int32)
    chosen = destination.reshape(tok_rows, top_k)[None, :, :] == slot_ids[:, None, None]
    placing = jnp.any(chosen, axis=2).astype(jnp.bfloat16)
    slotted = jnp.dot(placing, attended, preferred_element_type=jnp.float32).astype(
        jnp.bfloat16
    )
    slotted = jnp.repeat(slotted.reshape(EXPERTS, capacity, feat_local), copies, axis=0)
    outgoing = slotted.transpose(1, 0, 2).reshape(capacity, mp_count * feat_local)
    inbox_rows = lax.all_to_all(outgoing, MP, split_axis=1, concat_axis=1, tiled=True)
    stacked = lax.all_gather(jnp.stack([w_gate, w_up, w_down]), EX, axis=2, tiled=True)
    gate_next = jnp.einsum(
        "rd,hd->rh",
        inbox_rows,
        stacked[0],
        preferred_element_type=jnp.float32,
    )
    up_next = jnp.einsum(
        "rd,hd->rh",
        inbox_rows,
        stacked[1],
        preferred_element_type=jnp.float32,
    )
    activated = (jax.nn.silu(gate_next) * up_next).astype(jnp.bfloat16)
    partial_value = jnp.dot(
        activated,
        stacked[2],
        preferred_element_type=jnp.float32,
    )
    returned = lax.all_to_all(
        partial_value.astype(jnp.bfloat16), MP, split_axis=1, concat_axis=0, tiled=True
    )
    expert_out = jnp.sum(
        returned.reshape(EXPERTS, copies, capacity, feat_local).astype(jnp.float32), axis=1
    ).reshape(
        EXPERTS * capacity, feat_local
    )
    weights = 1.0 / (1.0 + jnp.exp(router_logits[:, ::-1] - router_logits))
    picking = jnp.sum(
        jnp.where(chosen, weights[None, :, :], 0.0), axis=2
    ).T
    branch = jnp.dot(
        picking, expert_out, precision=lax.Precision.HIGH, preferred_element_type=jnp.float32
    )
    combined = attended.astype(jnp.float32) + branch
    squares = jnp.sum(combined * combined, axis=1)
    squares = gather_sum(squares, MP)
    normed = (
        combined * norm_gain[None, :] * lax.rsqrt(squares / model_width + epsilon)[:, None]
    ).astype(jnp.bfloat16)
    ex_count = lax.axis_size(EX)
    everyone = lax.all_to_all(
        jnp.broadcast_to(normed[None], (ex_count,) + normed.shape),
        EX,
        split_axis=0,
        concat_axis=0,
        tiled=True,
    ).reshape(ex_count * tok_rows, feat_local)
    return everyone[request_order]


EX = ("ey", "ec")
MP = ("mx", "mz")


def split_mesh(mesh):
    devices = mesh.devices
    n_exp, n_mp = devices.shape
    row = devices[0].reshape(-1)
    try:
        z_count = len({d.coords[2] for d in row})
    except (AttributeError, IndexError, TypeError):
        z_count = n_mp
    return Mesh(
        devices.reshape(1, n_exp, n_mp // z_count, z_count), ("ey", "ec", "mx", "mz")
    )


def solution(mesh):
    fine = split_mesh(mesh)
    placed = (
        P(EX, MP),
        P(MP, None),
        P(EX, None),
        P(EX, None),
        P(MP, EX),
        P(MP, EX),
        P(MP, EX),
        P(MP),
        P(EX),
    )
    return jax.shard_map(
        shards, mesh=fine, in_specs=placed, out_specs=P(EX, MP), check_vma=False
    )
```

```python
import jax
import jax.numpy as jnp
from jax import lax
from jax.sharding import Mesh, PartitionSpec as P

EXPERTS = 8
CAP = 256


epsilon = 1e-06


def slot_targets(routes, capacity, experts):
    flat_routes = routes.reshape(-1)
    pairs = flat_routes.shape[0]
    onehot = (flat_routes[:, None] == jnp.arange(experts, dtype=jnp.int32)[None, :]).astype(
        jnp.bfloat16
    )
    order = jnp.arange(pairs, dtype=jnp.int32)
    before = (order[None, :] < order[:, None]).astype(jnp.bfloat16)
    earlier = jnp.dot(before, onehot, preferred_element_type=jnp.float32)
    slot_index = jnp.sum(earlier * onehot.astype(jnp.float32), axis=1).astype(jnp.int32)
    return flat_routes * capacity + slot_index


def gather_sum(values, axis):
    count = lax.axis_size(axis)
    spread = jnp.broadcast_to(values[None], (count,) + values.shape)
    return jnp.sum(lax.all_to_all(spread, axis, 0, 0, tiled=True), axis=0)


def shards(
    context, out_proj, routes, router_logits, w_gate, w_up, w_down, norm_gain, request_order
):
    tok_rows = context.shape[0]
    feat_local = context.shape[1]
    model_width = out_proj.shape[1]
    mp_count = lax.axis_size(MP)
    copies = mp_count // EXPERTS
    capacity = CAP
    top_k = routes.shape[1]
    x_count = lax.axis_size("mx")
    x_at = lax.axis_index("mx")
    along_z = lax.all_gather(context, "mz", axis=1, tiled=True)
    z_width = along_z.shape[1]
    rows_x = lax.all_to_all(
        jnp.broadcast_to(out_proj[None], (x_count,) + out_proj.shape),
        "mx",
        split_axis=0,
        concat_axis=0,
        tiled=True,
    ).reshape(x_count * feat_local, model_width)
    rows_x = lax.dynamic_slice_in_dim(rows_x, x_at * z_width, z_width, axis=1)
    partial_attended = jnp.einsum(
        "td,cd->tc", along_z, rows_x, preferred_element_type=jnp.float32
    )
    attended = jnp.sum(
        lax.all_to_all(
            partial_attended.reshape(tok_rows, x_count, feat_local),
            "mx",
            split_axis=1,
            concat_axis=1,
            tiled=True,
        ),
        axis=1,
    ).astype(jnp.bfloat16)
    destination = slot_targets(routes, capacity, EXPERTS)
    slot_ids = jnp.arange(EXPERTS * capacity, dtype=jnp.int32)
    chosen = destination.reshape(tok_rows, top_k)[None, :, :] == slot_ids[:, None, None]
    placing = jnp.any(chosen, axis=2).astype(jnp.bfloat16)
    slotted = jnp.dot(placing, attended, preferred_element_type=jnp.float32).astype(
        jnp.bfloat16
    )
    slotted = jnp.repeat(slotted.reshape(EXPERTS, capacity, feat_local), copies, axis=0)
    outgoing = slotted.transpose(1, 0, 2).reshape(capacity, mp_count * feat_local)
    inbox_rows = lax.all_to_all(outgoing, MP, split_axis=1, concat_axis=1, tiled=True)
    stacked = lax.all_gather(jnp.stack([w_gate, w_up, w_down]), EX, axis=2, tiled=True)
    both = jnp.einsum(
        "rd,ghd->rgh",
        inbox_rows,
        stacked[:2],
        preferred_element_type=jnp.float32,
    )
    gate_next = both[:, 0]
    up_next = both[:, 1]
    activated = (jax.nn.silu(gate_next) * up_next).astype(jnp.bfloat16)
    partial_value = jnp.dot(
        activated,
        stacked[2],
        preferred_element_type=jnp.float32,
    )
    returned = lax.all_to_all(
        partial_value.astype(jnp.bfloat16), MP, split_axis=1, concat_axis=0, tiled=True
    )
    expert_out = jnp.sum(
        returned.reshape(EXPERTS, copies, capacity, feat_local).astype(jnp.float32), axis=1
    ).reshape(
        EXPERTS * capacity, feat_local
    )
    weights = 1.0 / (1.0 + jnp.exp(router_logits[:, ::-1] - router_logits))
    picking = jnp.sum(
        jnp.where(chosen, weights[None, :, :], 0.0), axis=2
    ).T
    branch = jnp.dot(
        picking, expert_out, precision=lax.Precision.HIGH, preferred_element_type=jnp.float32
    )
    combined = attended.astype(jnp.float32) + branch
    squares = jnp.sum(combined * combined, axis=1)
    squares = gather_sum(squares, MP)
    normed = (
        combined * norm_gain[None, :] * lax.rsqrt(squares / model_width + epsilon)[:, None]
    ).astype(jnp.bfloat16)
    ex_count = lax.axis_size(EX)
    everyone = lax.all_to_all(
        jnp.broadcast_to(normed[None], (ex_count,) + normed.shape),
        EX,
        split_axis=0,
        concat_axis=0,
        tiled=True,
    ).reshape(ex_count * tok_rows, feat_local)
    return everyone[request_order]


EX = ("ey", "ec")
MP = ("mx", "mz")


def split_mesh(mesh):
    devices = mesh.devices
    n_exp, n_mp = devices.shape
    row = devices[0].reshape(-1)
    try:
        z_count = len({d.coords[2] for d in row})
    except (AttributeError, IndexError, TypeError):
        z_count = n_mp
    return Mesh(
        devices.reshape(1, n_exp, n_mp // z_count, z_count), ("ey", "ec", "mx", "mz")
    )


def solution(mesh):
    fine = split_mesh(mesh)
    placed = (
        P(EX, MP),
        P(MP, None),
        P(EX, None),
        P(EX, None),
        P(MP, EX),
        P(MP, EX),
        P(MP, EX),
        P(MP),
        P(EX),
    )
    return jax.shard_map(
        shards, mesh=fine, in_specs=placed, out_specs=P(EX, MP), check_vma=False
    )
```
